128 devices in a mesh: gr: 8 (over z_hi, x), gc: 16 (over y, z_lo, core).
Axes of the slice: x: 4, y: 4, z: 4 (z_hi: 2, z_lo: 2; z = z_hi * 2 + z_lo), core: 2. Of those that a mesh axis runs over, the one named last changes fastest.
Arguments:
- samples: bfloat16 [4096, 16384], P(('gr', 'gc')), may hold values from -6 to 6
- ridge: float32 [16384], replicated, may hold values from 1 to 4
Outputs:
- factored: float32 [8, 16, 128, 16, 8, 128], P('gr', None, None, 'gc')
The draws below stay inside these ranges and needn't reach their ends.
All inputs are finite; a program needn't handle non-finite values.
Results may differ from the reference program's by a relative error of at most 0.0003.
Values may be sent and summed in bfloat16 or wider, within the bound.
No kernel may reach another device: no remote copies, remote signals or barrier semaphores. Data moves between devices by JAX's collectives and lax.ppermute only.
A program may use at most 128 MiB of HBM per device.

```python
import math
import jax
import jax.numpy as jnp
from jax import lax

D = 16384
B = 128
P_SIZE = 512
NS = 4096
TR = 16
TC = 8
N_GR = 8
N_GC = 16


def block_scale(rng, dims, split, least, largest):
    loudness = 1.0
    for position, shards_of in split:
        draws = jax.random.uniform(jax.random.fold_in(jax.random.fold_in(rng, 6), position), (shards_of,), jnp.float32, least / len(split), largest / len(split))
        loudness = loudness * jnp.repeat(jnp.exp(draws), dims[position] // shards_of).reshape((-1,) + (1,) * (len(dims) - 1 - position))
    return loudness


def noise(own_key, dims, spread, bound, pieces=(), kind=jnp.bfloat16):
    drawn = jax.random.normal(own_key, dims, jnp.float32) * spread
    if len(pieces) > 0:
        drawn = block_scale(own_key, dims, pieces, -0.22, 0.18) * drawn
    return jnp.clip(drawn, min=-bound, max=bound).astype(kind)


def setup_inputs(seed: int = 0) -> dict:
    seeds = jax.random.split(jax.random.key(seed), 3)
    return {
        "samples": noise(seeds[0], (NS, D), 1.0, 6.0, ((0, 128),)),
        "ridge": jnp.clip(jnp.exp(jax.random.uniform(seeds[1], (D,), jnp.float32, math.log(1.0), math.log(4.0))), 1.0, 4.0),
    }


def reference(samples, ridge):
    count = samples.shape[0]
    cov = jnp.dot(samples.T.astype(jnp.float32), samples.astype(jnp.float32), preferred_element_type=jnp.float32) / count
    where_diag = jnp.arange(D)
    cov = cov.at[where_diag, where_diag].add(ridge)
    corner = cov[:P_SIZE, :P_SIZE]
    lower = jnp.linalg.cholesky(corner)
    inverse = jax.scipy.linalg.solve_triangular(lower, jnp.eye(P_SIZE, dtype=jnp.float32), lower=True)
    panel = jnp.dot(cov[:, :P_SIZE].astype(jnp.float32), inverse.T.astype(jnp.float32), precision=lax.Precision.HIGHEST, preferred_element_type=jnp.float32)
    trail = cov[P_SIZE:, P_SIZE:] - jnp.dot(panel[P_SIZE:].astype(jnp.float32), panel[P_SIZE:].T.astype(jnp.float32), precision=lax.Precision.HIGHEST, preferred_element_type=jnp.float32)
    cov = cov.at[P_SIZE:, P_SIZE:].set(trail)
    cov = cov.at[:, :P_SIZE].set(panel)
    return cov.reshape(TR, N_GR, B, TC, N_GC, B).transpose(1, 0, 2, 4, 3, 5)
```

```python
import jax
import jax.numpy as jnp
from jax import lax
from jax.sharding import PartitionSpec as P

B = 128
P_SIZE = 512


def inner_rows(left, right):
    return lax.dot_general(
        left, right, (((0,), (0,)), ((), ())), preferred_element_type=jnp.float32
    )


def exact_dot(left, right, dims):
    return lax.dot_general(
        left,
        right,
        (dims, ((), ())),
        precision=lax.Precision.HIGHEST,
        preferred_element_type=jnp.float32,
    )


def body(samples, ridge):
    row_id = lax.axis_index("gr")
    col_id = lax.axis_index("gc")
    n_rows = lax.axis_size("gr")
    n_cols = lax.axis_size("gc")
    per_dev, width = samples.shape
    tile_rows = width // (B * n_rows)
    tile_cols = width // (B * n_cols)
    total = per_dev * n_rows * n_cols

    head = lax.all_gather(samples[:, :P_SIZE], ("gc", "gr"), axis=0, tiled=True)

    row_slab = lax.all_to_all(
        samples.reshape(per_dev, tile_rows, n_rows, B),
        "gr",
        split_axis=2,
        concat_axis=0,
        tiled=True,
    ).reshape(n_rows * per_dev, tile_rows * B)
    col_slab = lax.all_to_all(
        samples.reshape(per_dev, tile_cols, n_cols, B),
        "gc",
        split_axis=2,
        concat_axis=0,
        tiled=True,
    ).reshape(n_cols, per_dev, tile_cols * B)
    rows_all = lax.all_gather(row_slab, "gc", axis=0, tiled=True)
    cols_all = lax.all_gather(col_slab, "gr", axis=1, tiled=False).reshape(
        total, tile_cols * B
    )

    row_feat = (
        (jnp.arange(tile_rows, dtype=jnp.int32)[:, None] * n_rows + row_id) * B
        + jnp.arange(B, dtype=jnp.int32)[None, :]
    ).reshape(-1)
    col_feat = (
        (jnp.arange(tile_cols, dtype=jnp.int32)[:, None] * n_cols + col_id) * B
        + jnp.arange(B, dtype=jnp.int32)[None, :]
    ).reshape(-1)
    head_feat = jnp.arange(P_SIZE, dtype=jnp.int32)
    ridge_rows = lax.dynamic_index_in_dim(
        ridge.reshape(tile_rows, n_rows, B), row_id, 1, keepdims=False
    ).reshape(-1)
    ridge_cols = lax.dynamic_index_in_dim(
        ridge.reshape(tile_cols, n_cols, B), col_id, 1, keepdims=False
    ).reshape(-1)
    ridge_head = ridge[:P_SIZE]

    corner = inner_rows(head, head) / total + jnp.where(
        head_feat[:, None] == head_feat[None, :], ridge_head[:, None], 0.0
    )
    lower = jnp.linalg.cholesky(corner)
    inverse = jax.scipy.linalg.solve_triangular(
        lower, jnp.eye(P_SIZE, dtype=jnp.float32), lower=True
    )

    cov = inner_rows(rows_all, cols_all) / total + jnp.where(
        row_feat[:, None] == col_feat[None, :], ridge_rows[:, None], 0.0
    )
    cov_rh = inner_rows(rows_all, head) / total + jnp.where(
        row_feat[:, None] == head_feat[None, :], ridge_rows[:, None], 0.0
    )
    cov_ch = inner_rows(cols_all, head) / total + jnp.where(
        col_feat[:, None] == head_feat[None, :], ridge_cols[:, None], 0.0
    )
    row_panel = exact_dot(cov_rh, inverse, ((1,), (1,)))
    col_panel = exact_dot(cov_ch, inverse, ((1,), (1,)))
    update = exact_dot(row_panel, col_panel, ((1,), (1,)))
    trailing = (row_feat >= P_SIZE)[:, None] & (col_feat >= P_SIZE)[None, :]
    result = jnp.where(trailing, cov - update, cov)
    panel_tiles = P_SIZE // B
    owner = jnp.minimum(col_id, panel_tiles - 1)
    panel_block = lax.dynamic_slice_in_dim(row_panel, owner * B, B, 1)
    first_block = jnp.where(col_id < panel_tiles, panel_block, result[:, :B])
    result = jnp.concatenate([first_block, result[:, B:]], axis=1)
    return result.reshape(1, tile_rows, B, 1, tile_cols, B)


def solution(mesh):
    in_specs = (P(("gr", "gc"), None), P())
    out_specs = P("gr", None, None, "gc", None, None)
    return jax.shard_map(body, mesh=mesh, in_specs=in_specs, out_specs=out_specs, check_vma=False)
```

```python
import jax
import jax.numpy as jnp
from jax import lax
from jax.sharding import PartitionSpec as P

B = 128
P_SIZE = 512


def inner_rows(left, right):
    return lax.dot_general(
        left, right, (((0,), (0,)), ((), ())), preferred_element_type=jnp.float32
    )


def exact_dot(left, right, dims):
    return lax.dot_general(
        left,
        right,
        (dims, ((), ())),
        precision=lax.Precision.HIGH,
        preferred_element_type=jnp.float32,
    )


def body(samples, ridge):
    row_id = lax.axis_index("gr")
    col_id = lax.axis_index("gc")
    n_rows = lax.axis_size("gr")
    n_cols = lax.axis_size("gc")
    per_dev, width = samples.shape
    tile_rows = width // (B * n_rows)
    tile_cols = width // (B * n_cols)
    total = per_dev * n_rows * n_cols

    head = lax.all_gather(
        lax.all_gather(samples[:, :P_SIZE], "gr", axis=0, tiled=True), "gc", axis=0, tiled=True
    )

    row_slab = lax.all_to_all(
        samples.reshape(per_dev, tile_rows, n_rows, B),
        "gr",
        split_axis=2,
        concat_axis=0,
        tiled=True,
    ).reshape(n_rows * per_dev, tile_rows * B)
    col_slab = lax.all_to_all(
        samples.reshape(per_dev, tile_cols, n_cols, B),
        "gc",
        split_axis=2,
        concat_axis=0,
        tiled=True,
    ).reshape(n_cols, per_dev, tile_cols * B)
    rows_all = lax.all_gather(row_slab, "gc", axis=0, tiled=True)
    cols_all = lax.all_gather(col_slab, "gr", axis=1, tiled=False).reshape(
        total, tile_cols * B
    )

    row_feat = (
        (jnp.arange(tile_rows, dtype=jnp.int32)[:, None] * n_rows + row_id) * B
        + jnp.arange(B, dtype=jnp.int32)[None, :]
    ).reshape(-1)
    col_feat = (
        (jnp.arange(tile_cols, dtype=jnp.int32)[:, None] * n_cols + col_id) * B
        + jnp.arange(B, dtype=jnp.int32)[None, :]
    ).reshape(-1)
    head_feat = jnp.arange(P_SIZE, dtype=jnp.int32)
    ridge_rows = lax.dynamic_index_in_dim(
        ridge.reshape(tile_rows, n_rows, B), row_id, 1, keepdims=False
    ).reshape(-1)
    ridge_cols = lax.dynamic_index_in_dim(
        ridge.reshape(tile_cols, n_cols, B), col_id, 1, keepdims=False
    ).reshape(-1)
    ridge_head = ridge[:P_SIZE]

    corner = inner_rows(head, head) / total + jnp.where(
        head_feat[:, None] == head_feat[None, :], ridge_head[:, None], 0.0
    )
    lower = jnp.linalg.cholesky(corner)
    inverse = jax.scipy.linalg.solve_triangular(
        lower, jnp.eye(P_SIZE, dtype=jnp.float32), lower=True
    )

    cov = inner_rows(rows_all, cols_all) / total + jnp.where(
        row_feat[:, None] == col_feat[None, :], ridge_rows[:, None], 0.0
    )
    cov_rh = inner_rows(rows_all, head) / total + jnp.where(
        row_feat[:, None] == head_feat[None, :], ridge_rows[:, None], 0.0
    )
    cov_ch = inner_rows(cols_all, head) / total + jnp.where(
        col_feat[:, None] == head_feat[None, :], ridge_cols[:, None], 0.0
    )
    row_panel = exact_dot(cov_rh, inverse, ((1,), (1,)))
    col_panel = exact_dot(cov_ch, inverse, ((1,), (1,)))
    update = exact_dot(row_panel, col_panel, ((1,), (1,)))
    trailing = (row_feat >= P_SIZE)[:, None] & (col_feat >= P_SIZE)[None, :]
    panel_tiles = P_SIZE // B
    owner = jnp.minimum(col_id, panel_tiles - 1)
    panel_block = lax.dynamic_slice_in_dim(row_panel, owner * B, B, 1)
    result = jnp.where(trailing, cov - update, cov)
    first_block = jnp.where(col_id < panel_tiles, panel_block, result[:, :B])
    result = lax.dynamic_update_slice(result, first_block, (0, 0))
    return result.reshape(1, tile_rows, B, 1, tile_cols, B)


def solution(mesh):
    in_specs = (P(("gr", "gc"), None), P())
    out_specs = P("gr", None, None, "gc", None, None)
    return jax.shard_map(body, mesh=mesh, in_specs=in_specs, out_specs=out_specs, check_vma=False)
```

```python
import jax
import jax.numpy as jnp
from jax import lax
from jax.sharding import PartitionSpec as P

B = 128
P_SIZE = 512


def inner_rows(left, right):
    return lax.dot_general(
        left, right, (((0,), (0,)), ((), ())), preferred_element_type=jnp.float32
    )


def exact_dot(left, right, dims):
    return lax.dot_general(
        left,
        right,
        (dims, ((), ())),
        precision=lax.Precision.HIGH,
        preferred_element_type=jnp.float32,
    )


def body(samples, ridge):
    row_id = lax.axis_index("gr")
    col_id = lax.axis_index("gc")
    n_rows = lax.axis_size("gr")
    n_cols = lax.axis_size("gc")
    per_dev, width = samples.shape
    tile_rows = width // (B * n_rows)
    tile_cols = width // (B * n_cols)
    total = per_dev * n_rows * n_cols

    feat_w = tile_rows * B
    send = jnp.concatenate(
        [
            samples.reshape(per_dev, tile_rows, n_rows, B).transpose(2, 0, 1, 3).reshape(
                n_rows, per_dev, feat_w
            ),
            jnp.broadcast_to(samples[None, :, :P_SIZE], (n_rows, per_dev, P_SIZE)),
        ],
        axis=2,
    )
    recv = lax.all_to_all(send, "gr", split_axis=0, concat_axis=0, tiled=True)
    row_slab = recv[:, :, :feat_w].reshape(n_rows * per_dev, feat_w)
    head_slab = recv[:, :, feat_w:].reshape(n_rows * per_dev, P_SIZE)
    head = lax.all_gather(head_slab, "gc", axis=0, tiled=True)

    col_slab = lax.all_to_all(
        samples.reshape(per_dev, tile_cols, n_cols, B),
        "gc",
        split_axis=2,
        concat_axis=0,
        tiled=True,
    ).reshape(n_cols, 1, per_dev, tile_cols * B)
    rows_all = lax.all_gather(row_slab, "gc", axis=0, tiled=True)
    cols_buf = jnp.zeros((n_cols, n_rows, per_dev, tile_cols * B), samples.dtype)
    for k in range(n_rows):
        if k == 0:
            part = col_slab
        else:
            part = lax.ppermute(
                col_slab, "gr", perm=[(i, (i + k) % n_rows) for i in range(n_rows)]
            )
        src = (row_id + (n_rows - k)) % n_rows
        cols_buf = lax.dynamic_update_slice(cols_buf, part, (0, src, 0, 0))
    cols_all = cols_buf.reshape(total, tile_cols * B)

    row_feat = (
        (jnp.arange(tile_rows, dtype=jnp.int32)[:, None] * n_rows + row_id) * B
        + jnp.arange(B, dtype=jnp.int32)[None, :]
    ).reshape(-1)
    col_feat = (
        (jnp.arange(tile_cols, dtype=jnp.int32)[:, None] * n_cols + col_id) * B
        + jnp.arange(B, dtype=jnp.int32)[None, :]
    ).reshape(-1)
    head_feat = jnp.arange(P_SIZE, dtype=jnp.int32)
    ridge_rows = lax.dynamic_index_in_dim(
        ridge.reshape(tile_rows, n_rows, B), row_id, 1, keepdims=False
    ).reshape(-1)
    ridge_cols = lax.dynamic_index_in_dim(
        ridge.reshape(tile_cols, n_cols, B), col_id, 1, keepdims=False
    ).reshape(-1)
    ridge_head = ridge[:P_SIZE]

    corner = inner_rows(head, head) / total + jnp.where(
        head_feat[:, None] == head_feat[None, :], ridge_head[:, None], 0.0
    )
    lower = jnp.linalg.cholesky(corner)
    inverse = jax.scipy.linalg.solve_triangular(
        lower, jnp.eye(P_SIZE, dtype=jnp.float32), lower=True
    )

    cov = inner_rows(rows_all, cols_all) / total + jnp.where(
        row_feat[:, None] == col_feat[None, :], ridge_rows[:, None], 0.0
    )
    cov_rh = inner_rows(rows_all, head) / total + jnp.where(
        row_feat[:, None] == head_feat[None, :], ridge_rows[:, None], 0.0
    )
    cov_ch = inner_rows(cols_all, head) / total + jnp.where(
        col_feat[:, None] == head_feat[None, :], ridge_cols[:, None], 0.0
    )
    row_panel = exact_dot(cov_rh, inverse, ((1,), (1,)))
    col_panel = exact_dot(cov_ch, inverse, ((1,), (1,)))
    update = exact_dot(row_panel, col_panel, ((1,), (1,)))
    trailing = (row_feat >= P_SIZE)[:, None] & (col_feat >= P_SIZE)[None, :]
    panel_tiles = P_SIZE // B
    owner = jnp.minimum(col_id, panel_tiles - 1)
    panel_block = lax.dynamic_slice_in_dim(row_panel, owner * B, B, 1)
    result = jnp.where(trailing, cov - update, cov)
    first_block = jnp.where(col_id < panel_tiles, panel_block, result[:, :B])
    result = lax.dynamic_update_slice(result, first_block, (0, 0))
    return result.reshape(1, tile_rows, B, 1, tile_cols, B)


def solution(mesh):
    in_specs = (P(("gr", "gc"), None), P())
    out_specs = P("gr", None, None, "gc", None, None)
    return jax.shard_map(body, mesh=mesh, in_specs=in_specs, out_specs=out_specs, check_vma=False)
```

```python
import jax
import jax.numpy as jnp
from jax import lax
from jax.sharding import Mesh, PartitionSpec as P

GC = ("gcy", "gcc")

B = 128
P_SIZE = 512


def inner_rows(left, right):
    return lax.dot_general(
        left, right, (((0,), (0,)), ((), ())), preferred_element_type=jnp.float32
    )


def exact_dot(left, right, dims):
    return lax.dot_general(
        left,
        right,
        (dims, ((), ())),
        precision=lax.Precision.HIGH,
        preferred_element_type=jnp.float32,
    )


def body(samples, ridge):
    row_id = lax.axis_index("gr")
    col_id = lax.axis_index(GC)
    n_rows = lax.axis_size("gr")
    n_cols = lax.axis_size("gcy") * lax.axis_size("gcc")
    per_dev, width = samples.shape
    tile_rows = width // (B * n_rows)
    tile_cols = width // (B * n_cols)
    total = per_dev * n_rows * n_cols

    feat_w = tile_rows * B
    send = jnp.concatenate(
        [
            samples.reshape(per_dev, tile_rows, n_rows, B).transpose(2, 0, 1, 3).reshape(
                n_rows, per_dev, feat_w
            ),
            jnp.broadcast_to(samples[None, :, :P_SIZE], (n_rows, per_dev, P_SIZE)),
        ],
        axis=2,
    )
    recv = lax.all_to_all(send, "gr", split_axis=0, concat_axis=0, tiled=True)
    row_slab = recv[:, :, :feat_w].reshape(n_rows * per_dev, feat_w)
    head_slab = recv[:, :, feat_w:].reshape(n_rows * per_dev, P_SIZE)

    def gather_gc(x):
        x = lax.all_gather(x, "gcy", axis=0, tiled=True)
        return lax.all_gather(x, "gcc", axis=0, tiled=True)

    n_chip = lax.axis_size("gcy")
    n_core = lax.axis_size("gcc")
    head = gather_gc(head_slab)

    col_slab = lax.all_to_all(
        samples.reshape(per_dev, tile_cols, n_cols, B),
        GC,
        split_axis=2,
        concat_axis=0,
        tiled=True,
    ).reshape(n_chip, n_core, per_dev, tile_cols * B)
    col_slab = col_slab.transpose(1, 0, 2, 3).reshape(n_core, n_chip, 1, per_dev, tile_cols * B)
    head, row_slab, col_slab = lax.optimization_barrier((head, row_slab, col_slab))
    rows_all = gather_gc(row_slab)
    cols_all = lax.all_gather(col_slab, "gr", axis=2, tiled=True).reshape(
        total, tile_cols * B
    )

    row_feat = (
        (jnp.arange(tile_rows, dtype=jnp.int32)[:, None] * n_rows + row_id) * B
        + jnp.arange(B, dtype=jnp.int32)[None, :]
    ).reshape(-1)
    col_feat = (
        (jnp.arange(tile_cols, dtype=jnp.int32)[:, None] * n_cols + col_id) * B
        + jnp.arange(B, dtype=jnp.int32)[None, :]
    ).reshape(-1)
    head_feat = jnp.arange(P_SIZE, dtype=jnp.int32)
    ridge_rows = lax.dynamic_index_in_dim(
        ridge.reshape(tile_rows, n_rows, B), row_id, 1, keepdims=False
    ).reshape(-1)
    ridge_cols = lax.dynamic_index_in_dim(
        ridge.reshape(tile_cols, n_cols, B), col_id, 1, keepdims=False
    ).reshape(-1)
    ridge_head = ridge[:P_SIZE]

    corner = inner_rows(head, head) / total + jnp.where(
        head_feat[:, None] == head_feat[None, :], ridge_head[:, None], 0.0
    )
    lower = jnp.linalg.cholesky(corner)
    inverse = jax.scipy.linalg.solve_triangular(
        lower, jnp.eye(P_SIZE, dtype=jnp.float32), lower=True
    )

    cov = inner_rows(rows_all, cols_all) / total + jnp.where(
        row_feat[:, None] == col_feat[None, :], ridge_rows[:, None], 0.0
    )
    cov_rh = inner_rows(rows_all, head) / total + jnp.where(
        row_feat[:, None] == head_feat[None, :], ridge_rows[:, None], 0.0
    )
    cov_ch = inner_rows(cols_all, head) / total + jnp.where(
        col_feat[:, None] == head_feat[None, :], ridge_cols[:, None], 0.0
    )
    row_panel = exact_dot(cov_rh, inverse, ((1,), (1,)))
    col_panel = exact_dot(cov_ch, inverse, ((1,), (1,)))
    update = exact_dot(row_panel, col_panel, ((1,), (1,)))
    trailing = (row_feat >= P_SIZE)[:, None] & (col_feat >= P_SIZE)[None, :]
    panel_tiles = P_SIZE // B
    owner = jnp.minimum(col_id, panel_tiles - 1)
    panel_block = lax.dynamic_slice_in_dim(row_panel, owner * B, B, 1)
    result = jnp.where(trailing, cov - update, cov)
    first_block = jnp.where(col_id < panel_tiles, panel_block, result[:, :B])
    result = lax.dynamic_update_slice(result, first_block, (0, 0))
    return result.reshape(1, tile_rows, B, 1, tile_cols, B)


def solution(mesh):
    n_core = 2
    devices = mesh.devices.reshape(mesh.shape["gr"], mesh.shape["gc"] // n_core, n_core)
    fine = Mesh(devices, ("gr", "gcy", "gcc"))
    in_specs = (P(("gr", "gcy", "gcc"), None), P())
    out_specs = P("gr", None, None, ("gcy", "gcc"), None, None)
    return jax.shard_map(body, mesh=fine, in_specs=in_specs, out_specs=out_specs, check_vma=False)
```

```python
import jax
import jax.numpy as jnp
from jax import lax
from jax.sharding import PartitionSpec as P

B = 128
P_SIZE = 512


def inner_rows(left, right):
    return lax.dot_general(
        left, right, (((0,), (0,)), ((), ())), preferred_element_type=jnp.float32
    )


def exact_dot(left, right, dims):
    return lax.dot_general(
        left,
        right,
        (dims, ((), ())),
        precision=lax.Precision.HIGH,
        preferred_element_type=jnp.float32,
    )


def body(samples, ridge):
    row_id = lax.axis_index("gr")
    col_id = lax.axis_index("gc")
    n_rows = lax.axis_size("gr")
    n_cols = lax.axis_size("gc")
    per_dev, width = samples.shape
    tile_rows = width // (B * n_rows)
    tile_cols = width // (B * n_cols)
    total = per_dev * n_rows * n_cols

    feat_w = tile_rows * B
    send = jnp.concatenate(
        [
            samples.reshape(per_dev, tile_rows, n_rows, B).transpose(2, 0, 1, 3).reshape(
                n_rows, per_dev, feat_w
            ),
            jnp.broadcast_to(samples[None, :, :P_SIZE], (n_rows, per_dev, P_SIZE)),
        ],
        axis=2,
    )
    recv = lax.all_to_all(send, "gr", split_axis=0, concat_axis=0, tiled=True)
    row_slab = recv[:, :, :feat_w].reshape(n_rows * per_dev, feat_w)
    head_slab = recv[:, :, feat_w:].reshape(n_rows * per_dev, P_SIZE)
    head = lax.all_gather(head_slab, "gc", axis=0, tiled=True)

    col_slab = lax.all_to_all(
        samples.reshape(per_dev, tile_cols, n_cols, B),
        "gc",
        split_axis=2,
        concat_axis=0,
        tiled=True,
    ).reshape(n_cols, per_dev, tile_cols * B)
    cols_all = lax.all_gather(col_slab, "gr", axis=1, tiled=False).reshape(
        total, tile_cols * B
    )

    row_feat = (
        (jnp.arange(tile_rows, dtype=jnp.int32)[:, None] * n_rows + row_id) * B
        + jnp.arange(B, dtype=jnp.int32)[None, :]
    ).reshape(-1)
    col_feat = (
        (jnp.arange(tile_cols, dtype=jnp.int32)[:, None] * n_cols + col_id) * B
        + jnp.arange(B, dtype=jnp.int32)[None, :]
    ).reshape(-1)
    head_feat = jnp.arange(P_SIZE, dtype=jnp.int32)
    ridge_rows = lax.dynamic_index_in_dim(
        ridge.reshape(tile_rows, n_rows, B), row_id, 1, keepdims=False
    ).reshape(-1)
    ridge_cols = lax.dynamic_index_in_dim(
        ridge.reshape(tile_cols, n_cols, B), col_id, 1, keepdims=False
    ).reshape(-1)
    ridge_head = ridge[:P_SIZE]

    corner = inner_rows(head, head) / total + jnp.where(
        head_feat[:, None] == head_feat[None, :], ridge_head[:, None], 0.0
    )
    lower = jnp.linalg.cholesky(corner)
    inverse = jax.scipy.linalg.solve_triangular(
        lower, jnp.eye(P_SIZE, dtype=jnp.float32), lower=True
    )

    cov_ch = inner_rows(cols_all, head) / total + jnp.where(
        col_feat[:, None] == head_feat[None, :], ridge_cols[:, None], 0.0
    )
    col_panel = exact_dot(cov_ch, inverse, ((1,), (1,)))
    panel_tiles = P_SIZE // B
    owner = jnp.minimum(col_id, panel_tiles - 1)

    n_piece = 2
    piece = feat_w // n_piece
    results = []
    for h in range(n_piece):
        rows_all = lax.all_gather(row_slab[:, h * piece:(h + 1) * piece], "gc", axis=0, tiled=True)
        feat_h = row_feat[h * piece:(h + 1) * piece]
        ridge_h = ridge_rows[h * piece:(h + 1) * piece]
        cov = inner_rows(rows_all, cols_all) / total + jnp.where(
            feat_h[:, None] == col_feat[None, :], ridge_h[:, None], 0.0
        )
        cov_rh = inner_rows(rows_all, head) / total + jnp.where(
            feat_h[:, None] == head_feat[None, :], ridge_h[:, None], 0.0
        )
        row_panel = exact_dot(cov_rh, inverse, ((1,), (1,)))
        update = exact_dot(row_panel, col_panel, ((1,), (1,)))
        trailing = (feat_h >= P_SIZE)[:, None] & (col_feat >= P_SIZE)[None, :]
        result = jnp.where(trailing, cov - update, cov)
        panel_block = lax.dynamic_slice_in_dim(row_panel, owner * B, B, 1)
        first_block = jnp.where(col_id < panel_tiles, panel_block, result[:, :B])
        results.append(lax.dynamic_update_slice(result, first_block, (0, 0)))
    result = jnp.concatenate(results, axis=0)
    return result.reshape(1, tile_rows, B, 1, tile_cols, B)


def solution(mesh):
    in_specs = (P(("gr", "gc"), None), P())
    out_specs = P("gr", None, None, "gc", None, None)
    return jax.shard_map(body, mesh=mesh, in_specs=in_specs, out_specs=out_specs, check_vma=False)
```

```python
import jax
import jax.numpy as jnp
from jax import lax
from jax.sharding import PartitionSpec as P


B = 128
P_SIZE = 512


def inner_rows(left, right):
    return lax.dot_general(
        left, right, (((0,), (0,)), ((), ())), preferred_element_type=jnp.float32
    )


def exact_dot(left, right, dims):
    return lax.dot_general(
        left,
        right,
        (dims, ((), ())),
        precision=lax.Precision.HIGH,
        preferred_element_type=jnp.float32,
    )


def steps(samples, ridge):
    row_id = lax.axis_index("gr")
    col_id = lax.axis_index("gc")
    n_rows = lax.axis_size("gr")
    n_cols = lax.axis_size("gc")
    per_dev, width = samples.shape
    tile_rows = width // (B * n_rows)
    tile_cols = width // (B * n_cols)
    total = per_dev * n_rows * n_cols

    feat_w = tile_rows * B
    send = jnp.concatenate(
        [
            samples.reshape(per_dev, tile_rows, n_rows, B).transpose(2, 0, 1, 3).reshape(
                n_rows, per_dev, feat_w
            ),
            jnp.broadcast_to(samples[None, :, :P_SIZE], (n_rows, per_dev, P_SIZE)),
        ],
        axis=2,
    )
    recv = lax.all_to_all(send, "gr", split_axis=0, concat_axis=0, tiled=True)
    row_slab = recv[:, :, :feat_w].reshape(n_rows * per_dev, feat_w)
    head_slab = recv[:, :, feat_w:].reshape(n_rows * per_dev, P_SIZE)
    head = lax.all_gather(head_slab, "gc", axis=0, tiled=True)

    col_slab = lax.all_to_all(
        samples.reshape(per_dev, tile_cols, n_cols, B),
        "gc",
        split_axis=2,
        concat_axis=0,
        tiled=True,
    ).reshape(n_cols, per_dev, tile_cols * B)
    cols_all = lax.all_gather(col_slab, "gr", axis=1, tiled=False).reshape(
        total, tile_cols * B
    )

    row_feat = (
        (jnp.arange(tile_rows, dtype=jnp.int32)[:, None] * n_rows + row_id) * B
        + jnp.arange(B, dtype=jnp.int32)[None, :]
    ).reshape(-1)
    col_feat = (
        (jnp.arange(tile_cols, dtype=jnp.int32)[:, None] * n_cols + col_id) * B
        + jnp.arange(B, dtype=jnp.int32)[None, :]
    ).reshape(-1)
    head_feat = jnp.arange(P_SIZE, dtype=jnp.int32)
    ridge_rows = lax.dynamic_index_in_dim(
        ridge.reshape(tile_rows, n_rows, B), row_id, 1, keepdims=False
    ).reshape(-1)
    ridge_cols = lax.dynamic_index_in_dim(
        ridge.reshape(tile_cols, n_cols, B), col_id, 1, keepdims=False
    ).reshape(-1)
    ridge_head = ridge[:P_SIZE]

    corner = inner_rows(head, head) / total + jnp.where(
        head_feat[:, None] == head_feat[None, :], ridge_head[:, None], 0.0
    )
    lower = jnp.linalg.cholesky(corner)
    inverse = jax.scipy.linalg.solve_triangular(
        lower, jnp.eye(P_SIZE, dtype=jnp.float32), lower=True
    )

    cov_ch = inner_rows(cols_all, head) / total + jnp.where(
        col_feat[:, None] == head_feat[None, :], ridge_cols[:, None], 0.0
    )
    col_panel = exact_dot(cov_ch, inverse, ((1,), (1,)))
    panel_tiles = P_SIZE // B
    owner = jnp.minimum(col_id, panel_tiles - 1)

    n_piece = 4
    piece = feat_w // n_piece
    results = []
    gathered = []
    for h in range(n_piece):
        gathered.append(
            lax.all_gather(row_slab[:, h * piece:(h + 1) * piece], "gc", axis=0, tiled=True)
        )
    for h in range(n_piece):
        rows_all = gathered[h]
        feat_h = row_feat[h * piece:(h + 1) * piece]
        ridge_h = ridge_rows[h * piece:(h + 1) * piece]
        cov = inner_rows(rows_all, cols_all) / total + jnp.where(
            feat_h[:, None] == col_feat[None, :], ridge_h[:, None], 0.0
        )
        cov_rh = inner_rows(rows_all, head) / total + jnp.where(
            feat_h[:, None] == head_feat[None, :], ridge_h[:, None], 0.0
        )
        row_panel = exact_dot(cov_rh, inverse, ((1,), (1,)))
        update = exact_dot(row_panel, col_panel, ((1,), (1,)))
        trailing = (feat_h >= P_SIZE)[:, None] & (col_feat >= P_SIZE)[None, :]
        result = jnp.where(trailing, cov - update, cov)
        panel_block = lax.dynamic_slice_in_dim(row_panel, owner * B, B, 1)
        first_block = jnp.where(col_id < panel_tiles, panel_block, result[:, :B])
        results.append(lax.dynamic_update_slice(result, first_block, (0, 0)))
    result = jnp.concatenate(results, axis=0)
    return result.reshape(1, tile_rows, B, 1, tile_cols, B)


def solution(mesh):
    in_specs = (P(("gr", "gc"), None), P())
    out_specs = P("gr", None, None, "gc", None, None)
    return jax.shard_map(steps, mesh=mesh, in_specs=in_specs, out_specs=out_specs, check_vma=False)
```

```python
import jax
import jax.numpy as jnp
from jax import lax
from jax.sharding import PartitionSpec as P


B = 128
P_SIZE = 512


def inner_rows(left, right):
    return lax.dot_general(
        left, right, (((0,), (0,)), ((), ())), preferred_element_type=jnp.float32
    )


def exact_dot(left, right, dims):
    return lax.dot_general(
        left,
        right,
        (dims, ((), ())),
        precision=lax.Precision.HIGH,
        preferred_element_type=jnp.float32,
    )


def steps(samples, ridge):
    row_id = lax.axis_index("gr")
    col_id = lax.axis_index("gc")
    n_rows = lax.axis_size("gr")
    n_cols = lax.axis_size("gc")
    per_dev, width = samples.shape
    tile_rows = width // (B * n_rows)
    tile_cols = width // (B * n_cols)
    total = per_dev * n_rows * n_cols

    feat_w = tile_rows * B
    head_own = samples[:, :P_SIZE].reshape(1, per_dev, P_SIZE)
    head_buf = jnp.zeros((n_rows, per_dev, P_SIZE), samples.dtype)
    for k in range(n_rows):
        if k == 0:
            part = head_own
        else:
            part = lax.ppermute(head_own, "gr", perm=[(i, (i + k) % n_rows) for i in range(n_rows)])
        src = (row_id + (n_rows - k)) % n_rows
        head_buf = lax.dynamic_update_slice(head_buf, part, (src, 0, 0))
    head_slab = head_buf.reshape(n_rows * per_dev, P_SIZE)
    row_slab = lax.all_to_all(
        samples.reshape(per_dev, tile_rows, n_rows, B),
        "gr",
        split_axis=2,
        concat_axis=0,
        tiled=True,
    ).reshape(n_rows * per_dev, feat_w)
    head = lax.all_gather(head_slab, "gc", axis=0, tiled=True)

    col_slab = lax.all_to_all(
        samples.reshape(per_dev, tile_cols, n_cols, B),
        "gc",
        split_axis=2,
        concat_axis=0,
        tiled=True,
    ).reshape(n_cols, per_dev, tile_cols * B)
    cols_all = lax.all_gather(col_slab, "gr", axis=1, tiled=False).reshape(
        total, tile_cols * B
    )

    row_feat = (
        (jnp.arange(tile_rows, dtype=jnp.int32)[:, None] * n_rows + row_id) * B
        + jnp.arange(B, dtype=jnp.int32)[None, :]
    ).reshape(-1)
    col_feat = (
        (jnp.arange(tile_cols, dtype=jnp.int32)[:, None] * n_cols + col_id) * B
        + jnp.arange(B, dtype=jnp.int32)[None, :]
    ).reshape(-1)
    head_feat = jnp.arange(P_SIZE, dtype=jnp.int32)
    ridge_rows = lax.dynamic_index_in_dim(
        ridge.reshape(tile_rows, n_rows, B), row_id, 1, keepdims=False
    ).reshape(-1)
    ridge_cols = lax.dynamic_index_in_dim(
        ridge.reshape(tile_cols, n_cols, B), col_id, 1, keepdims=False
    ).reshape(-1)
    ridge_head = ridge[:P_SIZE]

    corner = inner_rows(head, head) / total + jnp.where(
        head_feat[:, None] == head_feat[None, :], ridge_head[:, None], 0.0
    )
    lower = jnp.linalg.cholesky(corner)
    inverse = jax.scipy.linalg.solve_triangular(
        lower, jnp.eye(P_SIZE, dtype=jnp.float32), lower=True
    )

    cov_ch = inner_rows(cols_all, head) / total + jnp.where(
        col_feat[:, None] == head_feat[None, :], ridge_cols[:, None], 0.0
    )
    col_panel = exact_dot(cov_ch, inverse, ((1,), (1,)))
    panel_tiles = P_SIZE // B
    owner = jnp.minimum(col_id, panel_tiles - 1)

    n_piece = 2
    piece = feat_w // n_piece
    results = []
    gathered = []
    for h in range(n_piece):
        gathered.append(
            lax.all_gather(row_slab[:, h * piece:(h + 1) * piece], "gc", axis=0, tiled=True)
        )
    for h in range(n_piece):
        rows_all = gathered[h]
        feat_h = row_feat[h * piece:(h + 1) * piece]
        ridge_h = ridge_rows[h * piece:(h + 1) * piece]
        cov = inner_rows(rows_all, cols_all) / total + jnp.where(
            feat_h[:, None] == col_feat[None, :], ridge_h[:, None], 0.0
        )
        cov_rh = inner_rows(rows_all, head) / total + jnp.where(
            feat_h[:, None] == head_feat[None, :], ridge_h[:, None], 0.0
        )
        row_panel = exact_dot(cov_rh, inverse, ((1,), (1,)))
        update = exact_dot(row_panel, col_panel, ((1,), (1,)))
        trailing = (feat_h >= P_SIZE)[:, None] & (col_feat >= P_SIZE)[None, :]
        result = jnp.where(trailing, cov - update, cov)
        panel_block = lax.dynamic_slice_in_dim(row_panel, owner * B, B, 1)
        first_block = jnp.where(col_id < panel_tiles, panel_block, result[:, :B])
        results.append(lax.dynamic_update_slice(result, first_block, (0, 0)))
    result = jnp.concatenate(results, axis=0)
    return result.reshape(1, tile_rows, B, 1, tile_cols, B)


def solution(mesh):
    in_specs = (P(("gr", "gc"), None), P())
    out_specs = P("gr", None, None, "gc", None, None)
    return jax.shard_map(steps, mesh=mesh, in_specs=in_specs, out_specs=out_specs, check_vma=False)
```

```python
import jax
import jax.numpy as jnp
from jax import lax
from jax.sharding import PartitionSpec as P


B = 128
P_SIZE = 512


def inner_rows(left, right):
    return lax.dot_general(
        left, right, (((0,), (0,)), ((), ())), preferred_element_type=jnp.float32
    )


def exact_dot(left, right, dims):
    return lax.dot_general(
        left,
        right,
        (dims, ((), ())),
        precision=lax.Precision.HIGH,
        preferred_element_type=jnp.float32,
    )


def steps(samples, ridge):
    row_id = lax.axis_index("gr")
    col_id = lax.axis_index("gc")
    n_rows = lax.axis_size("gr")
    n_cols = lax.axis_size("gc")
    per_dev, width = samples.shape
    tile_rows = width // (B * n_rows)
    tile_cols = width // (B * n_cols)
    total = per_dev * n_rows * n_cols

    feat_w = tile_rows * B
    send = jnp.concatenate(
        [
            samples.reshape(per_dev, tile_rows, n_rows, B).transpose(2, 0, 1, 3).reshape(
                n_rows, per_dev, feat_w
            ),
            jnp.broadcast_to(samples[None, :, :P_SIZE], (n_rows, per_dev, P_SIZE)),
        ],
        axis=2,
    )
    recv = lax.all_to_all(send, "gr", split_axis=0, concat_axis=0, tiled=True)
    row_slab = recv[:, :, :feat_w].reshape(n_rows * per_dev, feat_w)
    head_slab = recv[:, :, feat_w:].reshape(n_rows * per_dev, P_SIZE)
    head = lax.all_gather(head_slab, "gc", axis=0, tiled=True)

    col_slab = lax.all_to_all(
        samples.reshape(per_dev, tile_cols, n_cols, B),
        "gc",
        split_axis=2,
        concat_axis=0,
        tiled=True,
    ).reshape(n_cols, per_dev, tile_cols * B)
    cols_all = lax.all_gather(col_slab, "gr", axis=1, tiled=False).reshape(
        total, tile_cols * B
    )

    row_feat = (
        (jnp.arange(tile_rows, dtype=jnp.int32)[:, None] * n_rows + row_id) * B
        + jnp.arange(B, dtype=jnp.int32)[None, :]
    ).reshape(-1)
    col_feat = (
        (jnp.arange(tile_cols, dtype=jnp.int32)[:, None] * n_cols + col_id) * B
        + jnp.arange(B, dtype=jnp.int32)[None, :]
    ).reshape(-1)
    head_feat = jnp.arange(P_SIZE, dtype=jnp.int32)
    ridge_rows = lax.dynamic_index_in_dim(
        ridge.reshape(tile_rows, n_rows, B), row_id, 1, keepdims=False
    ).reshape(-1)
    ridge_cols = lax.dynamic_index_in_dim(
        ridge.reshape(tile_cols, n_cols, B), col_id, 1, keepdims=False
    ).reshape(-1)
    ridge_head = ridge[:P_SIZE]

    corner = inner_rows(head, head) / total + jnp.where(
        head_feat[:, None] == head_feat[None, :], ridge_head[:, None], 0.0
    )
    lower = jnp.linalg.cholesky(corner)
    inverse = jax.scipy.linalg.solve_triangular(
        lower, jnp.eye(P_SIZE, dtype=jnp.float32), lower=True
    )

    cov_ch = inner_rows(cols_all, head) / total + jnp.where(
        col_feat[:, None] == head_feat[None, :], ridge_cols[:, None], 0.0
    )
    col_panel = exact_dot(cov_ch, inverse, ((1,), (1,)))
    panel_tiles = P_SIZE // B
    owner = jnp.minimum(col_id, panel_tiles - 1)

    n_piece = 2
    piece = feat_w // n_piece
    results = []
    gathered = []
    for h in range(n_piece):
        gathered.append(
            lax.all_gather(row_slab[:, h * piece:(h + 1) * piece], "gc", axis=0, tiled=True)
        )
    for h in range(n_piece):
        rows_all = gathered[h]
        feat_h = row_feat[h * piece:(h + 1) * piece]
        ridge_h = ridge_rows[h * piece:(h + 1) * piece]
        cov = inner_rows(rows_all, cols_all) / total + jnp.where(
            feat_h[:, None] == col_feat[None, :], ridge_h[:, None], 0.0
        )
        cov_rh = inner_rows(rows_all, head) / total + jnp.where(
            feat_h[:, None] == head_feat[None, :], ridge_h[:, None], 0.0
        )
        row_panel = exact_dot(cov_rh, inverse, ((1,), (1,)))
        update = exact_dot(row_panel, col_panel, ((1,), (1,)))
        trailing = (feat_h >= P_SIZE)[:, None] & (col_feat >= P_SIZE)[None, :]
        result = jnp.where(trailing, cov - update, cov)
        panel_block = lax.dynamic_slice_in_dim(row_panel, owner * B, B, 1)
        first_block = jnp.where(col_id < panel_tiles, panel_block, result[:, :B])
        result = lax.dynamic_update_slice(result, first_block, (0, 0))
        results.append(result.reshape(1, tile_rows // n_piece, B, 1, tile_cols, B))
    return jnp.concatenate(results, axis=1)


def solution(mesh):
    in_specs = (P(("gr", "gc"), None), P())
    out_specs = P("gr", None, None, "gc", None, None)
    return jax.shard_map(steps, mesh=mesh, in_specs=in_specs, out_specs=out_specs, check_vma=False)
```

```python
import jax
import jax.numpy as jnp
from jax import lax
from jax.sharding import PartitionSpec as P


B = 128
P_SIZE = 512


def inner_rows(left, right):
    return lax.dot_general(
        left, right, (((0,), (0,)), ((), ())), preferred_element_type=jnp.float32
    )


def exact_dot(left, right, dims):
    return lax.dot_general(
        left,
        right,
        (dims, ((), ())),
        precision=lax.Precision.HIGH,
        preferred_element_type=jnp.float32,
    )


def steps(samples, ridge):
    row_id = lax.axis_index("gr")
    col_id = lax.axis_index("gc")
    n_rows = lax.axis_size("gr")
    n_cols = lax.axis_size("gc")
    per_dev, width = samples.shape
    tile_rows = width // (B * n_rows)
    tile_cols = width // (B * n_cols)
    total = per_dev * n_rows * n_cols

    feat_w = tile_rows * B
    send = jnp.concatenate(
        [
            samples.reshape(per_dev, tile_rows, n_rows, B).transpose(2, 0, 1, 3).reshape(
                n_rows, per_dev, feat_w
            ),
            jnp.broadcast_to(samples[None, :, :P_SIZE], (n_rows, per_dev, P_SIZE)),
        ],
        axis=2,
    )
    recv = lax.all_to_all(send, "gr", split_axis=0, concat_axis=0, tiled=True)
    row_slab = recv[:, :, :feat_w].reshape(n_rows * per_dev, feat_w)
    head_slab = recv[:, :, feat_w:].reshape(n_rows * per_dev, P_SIZE)
    head = lax.all_gather(head_slab, "gc", axis=0, tiled=True)

    col_slab = lax.all_to_all(
        samples.reshape(per_dev, tile_cols, n_cols, B),
        "gc",
        split_axis=2,
        concat_axis=0,
        tiled=True,
    ).reshape(n_cols, per_dev, tile_cols * B)
    cols_all = lax.all_gather(col_slab, "gr", axis=1, tiled=False).reshape(
        total, tile_cols * B
    )

    row_feat = (
        (jnp.arange(tile_rows, dtype=jnp.int32)[:, None] * n_rows + row_id) * B
        + jnp.arange(B, dtype=jnp.int32)[None, :]
    ).reshape(-1)
    col_feat = (
        (jnp.arange(tile_cols, dtype=jnp.int32)[:, None] * n_cols + col_id) * B
        + jnp.arange(B, dtype=jnp.int32)[None, :]
    ).reshape(-1)
    head_feat = jnp.arange(P_SIZE, dtype=jnp.int32)
    ridge_rows = lax.dynamic_index_in_dim(
        ridge.reshape(tile_rows, n_rows, B), row_id, 1, keepdims=False
    ).reshape(-1)
    ridge_cols = lax.dynamic_index_in_dim(
        ridge.reshape(tile_cols, n_cols, B), col_id, 1, keepdims=False
    ).reshape(-1)
    ridge_head = ridge[:P_SIZE]

    corner = inner_rows(head, head) / total + jnp.where(
        head_feat[:, None] == head_feat[None, :], ridge_head[:, None], 0.0
    )
    lower = jnp.linalg.cholesky(corner)
    inverse = jax.scipy.linalg.solve_triangular(
        lower, jnp.eye(P_SIZE, dtype=jnp.float32), lower=True
    )

    cov_ch = inner_rows(cols_all, head) / total + jnp.where(
        col_feat[:, None] == head_feat[None, :], ridge_cols[:, None], 0.0
    )
    col_panel = exact_dot(cov_ch, inverse, ((1,), (1,)))
    panel_tiles = P_SIZE // B
    owner = jnp.minimum(col_id, panel_tiles - 1)

    n_piece = 2
    first_tiles = (tile_rows * 10) // 16
    bounds = [0, first_tiles * B, feat_w]
    results = []
    gathered = []
    for h in range(n_piece):
        gathered.append(
            lax.all_gather(row_slab[:, bounds[h]:bounds[h + 1]], "gc", axis=0, tiled=True)
        )
    for h in range(n_piece):
        rows_all = gathered[h]
        feat_h = row_feat[bounds[h]:bounds[h + 1]]
        ridge_h = ridge_rows[bounds[h]:bounds[h + 1]]
        cov = inner_rows(rows_all, cols_all) / total + jnp.where(
            feat_h[:, None] == col_feat[None, :], ridge_h[:, None], 0.0
        )
        cov_rh = inner_rows(rows_all, head) / total + jnp.where(
            feat_h[:, None] == head_feat[None, :], ridge_h[:, None], 0.0
        )
        row_panel = exact_dot(cov_rh, inverse, ((1,), (1,)))
        update = exact_dot(row_panel, col_panel, ((1,), (1,)))
        trailing = (feat_h >= P_SIZE)[:, None] & (col_feat >= P_SIZE)[None, :]
        result = jnp.where(trailing, cov - update, cov)
        panel_block = lax.dynamic_slice_in_dim(row_panel, owner * B, B, 1)
        first_block = jnp.where(col_id < panel_tiles, panel_block, result[:, :B])
        result = lax.dynamic_update_slice(result, first_block, (0, 0))
        results.append(result.reshape(1, -1, B, 1, tile_cols, B))
    return jnp.concatenate(results, axis=1)


def solution(mesh):
    in_specs = (P(("gr", "gc"), None), P())
    out_specs = P("gr", None, None, "gc", None, None)
    return jax.shard_map(steps, mesh=mesh, in_specs=in_specs, out_specs=out_specs, check_vma=False)
```

```python
import jax
import jax.numpy as jnp
from jax import lax
from jax.sharding import PartitionSpec as P


B = 128
P_SIZE = 512


def inner_rows(left, right):
    return lax.dot_general(
        left, right, (((0,), (0,)), ((), ())), preferred_element_type=jnp.float32
    )


def exact_dot(left, right, dims):
    return lax.dot_general(
        left,
        right,
        (dims, ((), ())),
        precision=lax.Precision.HIGH,
        preferred_element_type=jnp.float32,
    )


def steps(samples, ridge):
    row_id = lax.axis_index("gr")
    col_id = lax.axis_index("gc")
    n_rows = lax.axis_size("gr")
    n_cols = lax.axis_size("gc")
    per_dev, width = samples.shape
    tile_rows = width // (B * n_rows)
    tile_cols = width // (B * n_cols)
    total = per_dev * n_rows * n_cols

    feat_w = tile_rows * B
    send = jnp.concatenate(
        [
            samples.reshape(per_dev, tile_rows, n_rows, B).transpose(2, 0, 1, 3).reshape(
                n_rows, per_dev, feat_w
            ),
            jnp.broadcast_to(samples[None, :, :P_SIZE], (n_rows, per_dev, P_SIZE)),
        ],
        axis=2,
    )
    recv = lax.all_to_all(send, "gr", split_axis=0, concat_axis=0, tiled=True)
    row_slab = recv[:, :, :feat_w].reshape(n_rows * per_dev, feat_w)
    head_slab = recv[:, :, feat_w:].reshape(n_rows * per_dev, P_SIZE)
    head = lax.all_gather(head_slab, "gc", axis=0, tiled=True)

    col_slab = lax.all_to_all(
        samples.reshape(per_dev, tile_cols, n_cols, B),
        "gc",
        split_axis=2,
        concat_axis=0,
        tiled=True,
    ).reshape(n_cols, per_dev, tile_cols * B)
    cols_all = lax.all_gather(col_slab, "gr", axis=1, tiled=False).reshape(
        total, tile_cols * B
    )

    row_feat = (
        (jnp.arange(tile_rows, dtype=jnp.int32)[:, None] * n_rows + row_id) * B
        + jnp.arange(B, dtype=jnp.int32)[None, :]
    ).reshape(-1)
    col_feat = (
        (jnp.arange(tile_cols, dtype=jnp.int32)[:, None] * n_cols + col_id) * B
        + jnp.arange(B, dtype=jnp.int32)[None, :]
    ).reshape(-1)
    head_feat = jnp.arange(P_SIZE, dtype=jnp.int32)
    ridge_rows = lax.dynamic_index_in_dim(
        ridge.reshape(tile_rows, n_rows, B), row_id, 1, keepdims=False
    ).reshape(-1)
    ridge_cols = lax.dynamic_index_in_dim(
        ridge.reshape(tile_cols, n_cols, B), col_id, 1, keepdims=False
    ).reshape(-1)
    ridge_head = ridge[:P_SIZE]

    corner = inner_rows(head, head) / total + jnp.where(
        head_feat[:, None] == head_feat[None, :], ridge_head[:, None], 0.0
    )
    lower = jnp.linalg.cholesky(corner)
    inverse = jax.scipy.linalg.solve_triangular(
        lower, jnp.eye(P_SIZE, dtype=jnp.float32), lower=True
    )

    cov_ch = inner_rows(cols_all, head) / total + jnp.where(
        col_feat[:, None] == head_feat[None, :], ridge_cols[:, None], 0.0
    )
    col_panel = exact_dot(cov_ch, inverse, ((1,), (1,)))
    panel_tiles = P_SIZE // B
    owner = jnp.minimum(col_id, panel_tiles - 1)

    col_w = tile_cols * B
    right_all = jnp.concatenate([cols_all, head], axis=1)
    n_piece = 2
    first_tiles = (tile_rows * 10) // 16
    bounds = [0, first_tiles * B, feat_w]
    results = []
    gathered = []
    for h in range(n_piece):
        gathered.append(
            lax.all_gather(row_slab[:, bounds[h]:bounds[h + 1]], "gc", axis=0, tiled=True)
        )
    for h in range(n_piece):
        rows_all = gathered[h]
        feat_h = row_feat[bounds[h]:bounds[h + 1]]
        ridge_h = ridge_rows[bounds[h]:bounds[h + 1]]
        both = inner_rows(rows_all, right_all) / total
        cov = both[:, :col_w] + jnp.where(
            feat_h[:, None] == col_feat[None, :], ridge_h[:, None], 0.0
        )
        cov_rh = both[:, col_w:] + jnp.where(
            feat_h[:, None] == head_feat[None, :], ridge_h[:, None], 0.0
        )
        row_panel = exact_dot(cov_rh, inverse, ((1,), (1,)))
        update = exact_dot(row_panel, col_panel, ((1,), (1,)))
        trailing = (feat_h >= P_SIZE)[:, None] & (col_feat >= P_SIZE)[None, :]
        result = jnp.where(trailing, cov - update, cov)
        panel_block = lax.dynamic_slice_in_dim(row_panel, owner * B, B, 1)
        first_block = jnp.where(col_id < panel_tiles, panel_block, result[:, :B])
        result = lax.dynamic_update_slice(result, first_block, (0, 0))
        results.append(result.reshape(1, -1, B, 1, tile_cols, B))
    return jnp.concatenate(results, axis=1)


def solution(mesh):
    in_specs = (P(("gr", "gc"), None), P())
    out_specs = P("gr", None, None, "gc", None, None)
    return jax.shard_map(steps, mesh=mesh, in_specs=in_specs, out_specs=out_specs, check_vma=False)
```
